256 devices in a mesh: dp: 16 (over z_hi, y, core), tensor: 16 (over z_lo, x).
Axes of the slice: x: 4, y: 4, z: 8 (z_hi: 2, z_lo: 4; z = z_hi * 4 + z_lo), core: 2. Of those that a mesh axis runs over, the one named last changes fastest.
Arguments:
- hidden: bfloat16 [4096, 14336], P('dp', 'tensor'), may hold values from -6 to 6
- residual: bfloat16 [4096, 8192], P('tensor', 'dp'), may hold values from -6 to 6
- master: float32 [14336, 8192], P('tensor', 'dp'), may hold values from -0.046875 to 0.046875
- moment: float32 [14336, 8192], P('tensor', 'dp'), may hold values from -0.00021362305 to 0.00021362305
- second: float32 [14336, 8192], P('tensor', 'dp'), as said below
- gain: float32 [8192], P('dp'), may hold values from 0.5 to 1.5
- head: float32 [8192], P('dp')
- lengths: int32 [16, 2], replicated, may hold values from 32 to 128, as said below
- labels: int32 [16], replicated, may hold values from 0 to 1
Outputs:
- new_master: float32 [14336, 8192], P('tensor', 'dp')
- new_moment: float32 [14336, 8192], P('tensor', 'dp')
- new_second: float32 [14336, 8192], P('tensor', 'dp')
- loss: float32 [], replicated
The draws below stay inside these ranges and needn't reach their ends.
Inputs may be any that keep to these rules, and one draw needn't show every extreme that they name: `lengths`: some sequence has exactly 128 valid tokens in every draw; every sequence has at least 32. `second`: Positive.
All inputs are finite; a program needn't handle non-finite values.
Results may differ from the reference program's by a relative error of at most 0.015.
Values may be sent and summed in bfloat16 or wider, within the bound.
No kernel may reach another device: no remote copies, remote signals or barrier semaphores. Data moves between devices by JAX's collectives and lax.ppermute only.
A program may use at most 128 MiB of HBM per device.

```python
import jax
import jax.numpy as jnp
from jax import lax

D = 8192
FF = 14336
LEN = 128
STEP = 100
PAIRS = 16
TOKENS = 4096
N_TENSOR = 16


def draw_lengths(key, part):
    first_key, second_key = jax.random.split(key)
    values = jax.random.randint(first_key, (PAIRS * 2,), LEN // 4, LEN + 1)
    where_full = jax.random.randint(second_key, (), 0, PAIRS * 2)
    values = jnp.where(jnp.arange(PAIRS * 2) == where_full, LEN, values)
    return values.reshape(PAIRS, 2).astype(jnp.int32)


def head_pattern(key):
    sub_key = jax.random.fold_in(key, 11)
    pattern = jnp.clip(jax.random.normal(sub_key, (D,), jnp.float32), -4.0, 4.0)
    return pattern


def draw_head(key, part):
    return (head_pattern(key) * (16.0 / D)).astype(jnp.float32)


def draw_residual(key, part):
    pattern = head_pattern(key)
    noise_key = jax.random.fold_in(key, 23)
    along_key = jax.random.fold_in(key, 37)
    noise = jnp.clip(jax.random.normal(noise_key, (TOKENS, D), jnp.float32), -4.0, 4.0)
    along = jax.random.uniform(along_key, (TOKENS, 1), jnp.float32, -0.8, 0.8)
    values = jnp.clip(noise + along * pattern[None, :], -6.0, 6.0)
    return values.astype(jnp.bfloat16)


def draw_second(key, part):
    sub_key = jax.random.fold_in(key, 5)
    logs = jax.random.uniform(sub_key, (FF, D), jnp.float32, jnp.log(0.3), jnp.log(3.0))
    return (jnp.exp(logs) / (float(D) * float(D))).astype(jnp.float32)


def place_ends(array, rng, low, high):
    shape = array.shape
    index_at = [jax.random.randint(jax.random.fold_in(rng, axis), (), 0, shape[axis]) for axis in range(len(shape))]
    array = array.at[tuple(index_at)].set(low)
    longest = shape.index(max(shape))
    index_at[longest] = (index_at[longest] + 1) % shape[longest]
    return array.at[tuple(index_at)].set(high)


def steps_of(rng, extent, shards, least, high):
    factor_of, own = 1.0, jax.random.fold_in(rng, 6)
    for axis_at, blocks in shards:
        heights = jnp.exp(jax.random.uniform(jax.random.fold_in(own, axis_at), (blocks,), jnp.float32, least / len(shards), high / len(shards)))
        factor_of = factor_of * jnp.repeat(heights, extent[axis_at] // blocks).reshape([-1 if axis == axis_at else 1 for axis in range(len(extent))])
    return factor_of


def gaussian(stream_key, extent, width, bound, cuts=(), dtype=jnp.bfloat16):
    entries = width * jax.random.normal(stream_key, extent, jnp.float32)
    if cuts:
        entries = entries * steps_of(stream_key, extent, cuts, -0.22, 0.18)
    return jnp.clip(entries, -bound, bound).astype(dtype)


def setup_inputs(seed: int = 0) -> dict:
    keys = jax.random.split(jax.random.key(seed), 10)
    hidden = gaussian(keys[0], (TOKENS, FF), 1.0, 6.0, ((0, 16), (1, 16)))
    residual = draw_residual(jax.random.fold_in(keys[9], 71), 0)
    master = gaussian(keys[2], (FF, D), FF ** -0.5, 0.046875, ((0, 16), (1, 16)), jnp.float32)
    moment = gaussian(keys[3], (FF, D), (11 * D * D) ** -0.5, 0.00021362305, ((0, 16), (1, 16)), jnp.float32)
    second = draw_second(jax.random.fold_in(keys[9], 71), 0)
    gain = jnp.clip(1.0 + 0.1 * jax.random.normal(keys[5], (D,), jnp.float32), 0.5, 1.5)
    head = draw_head(jax.random.fold_in(keys[9], 71), 0)
    lengths = draw_lengths(jax.random.fold_in(keys[9], 71), 0)
    labels = place_ends(jax.random.randint(keys[8], (PAIRS,), 0, 2), jax.random.fold_in(keys[8], 1), 0, 1).astype(jnp.int32)
    return {"hidden": hidden, "residual": residual, "master": master, "moment": moment, "second": second, "gain": gain, "head": head, "lengths": lengths, "labels": labels}


EPS_NORM = 1e-05

def reference(hidden, residual, master, moment, second, gain, head, lengths, labels):
    weights = master.astype(jnp.bfloat16)
    block_ff = FF // N_TENSOR
    block_rows = TOKENS // N_TENSOR
    resid = residual.astype(jnp.float32)

    def add_block(total, index):
        cols = lax.dynamic_slice_in_dim(hidden, index * block_ff, block_ff, 1)
        wrows = lax.dynamic_slice_in_dim(weights, index * block_ff, block_ff, 0)
        part = jnp.dot(cols, wrows, preferred_element_type=jnp.float32)
        own = lax.dynamic_slice_in_dim(part, index * block_rows, block_rows, 0)
        own = own + lax.dynamic_slice_in_dim(resid, index * block_rows, block_rows, 0)
        part = lax.dynamic_update_slice_in_dim(part, own, index * block_rows, 0)
        rounded = lax.optimization_barrier(part.astype(jnp.bfloat16))
        return (total + rounded.astype(jnp.float32), None)
    stream, _ = lax.scan(add_block, jnp.zeros((TOKENS, D), jnp.float32), jnp.arange(N_TENSOR).astype(jnp.int32))
    w_vec = gain * head
    row_ids = jnp.arange(TOKENS).astype(jnp.int32)
    seq_ids = row_ids // LEN
    pos = row_ids % LEN
    lens_flat = lengths.reshape(-1)
    len_row = lens_flat[seq_ids]
    valid = pos < len_row
    ss = lax.optimization_barrier(jnp.sum(stream * stream, 1))
    hy = lax.optimization_barrier(jnp.sum(stream * w_vec[None, :], 1))
    rstd = lax.rsqrt(ss / D + EPS_NORM)
    score = rstd * hy
    seq_total = jax.ops.segment_sum(jnp.where(valid, score, 0.0), seq_ids, 2 * PAIRS)
    reward = (seq_total / lens_flat.astype(jnp.float32)).reshape(PAIRS, 2)
    chosen = jnp.where(labels == 1, reward[:, 1], reward[:, 0])
    other = jnp.where(labels == 1, reward[:, 0], reward[:, 1])
    margin = chosen - other
    loss = jnp.sum(jax.nn.softplus(-margin))
    sig = jax.nn.sigmoid(-margin)
    first = jnp.where(labels == 0, -sig, sig)
    dreward = jnp.stack([first, -first], 1).reshape(-1)
    coef = jnp.where(valid, dreward[seq_ids] / len_row.astype(jnp.float32), 0.0)
    cotangent = (coef[:, None] * (rstd[:, None] * w_vec[None, :] - (hy * rstd ** 3 / D)[:, None] * stream)).astype(jnp.bfloat16)
    grad = jnp.dot(hidden.T, cotangent, preferred_element_type=jnp.float32)
    new_moment = 0.9 * moment + 0.1 * grad
    new_second = 0.95 * second + 0.05 * grad * grad
    m_hat = new_moment / (1.0 - 0.9 ** STEP)
    v_hat = new_second / (1.0 - 0.95 ** STEP)
    new_master = master - 0.001 * (m_hat / (jnp.sqrt(v_hat) + 1e-08) + 0.1 * master)
    return (new_master, new_moment, new_second, loss)
```

```python
import jax
import jax.numpy as jnp
import numpy as np
from jax import lax
from jax.sharding import Mesh
from jax.sharding import PartitionSpec as P

D = 8192
LEN = 128
STEP = 100


EPS_NORM = 1e-05

DP_PARTS = (("z_hi", 2), ("y", 4), ("core", 2))
TP_PARTS = (("z_lo", 4), ("x", 4))
DP_AXES = tuple(name for name, _ in DP_PARTS)
TP_AXES = tuple(name for name, _ in TP_PARTS)


def psum_steps(value, axes):
    for axis in reversed(axes):
        value = lax.psum(value, axis)
    return value


def per_device(hidden, residual, master, moment, second, gain, head, lengths, labels):
    t_index = lax.axis_index(TP_AXES)
    block_rows = residual.shape[0]
    weights = master.astype(jnp.bfloat16)
    gathered = lax.all_gather(hidden, DP_AXES, axis=0, tiled=True)
    partial_value = jnp.dot(gathered, weights, preferred_element_type=jnp.float32)
    row_start = t_index * block_rows
    own = lax.dynamic_slice_in_dim(partial_value, row_start, block_rows, 0) + residual.astype(
        jnp.float32
    )
    term = lax.dynamic_update_slice_in_dim(partial_value, own, row_start, 0)
    w_vec = gain * head
    stream = lax.psum_scatter(
        term.astype(jnp.bfloat16), TP_AXES, scatter_dimension=0, tiled=True
    ).astype(jnp.float32)
    squares = jnp.sum(stream * stream, 1)
    product = jnp.sum(stream * w_vec[None, :], 1)
    squares, product = psum_steps((squares, product), DP_AXES)

    seqs_here = block_rows // LEN
    pairs_here = seqs_here // 2
    lens_flat = lengths.reshape(-1)
    lens_here = lax.dynamic_slice_in_dim(lens_flat, t_index * seqs_here, seqs_here, 0)
    labels_here = lax.dynamic_slice_in_dim(labels, t_index * pairs_here, pairs_here, 0)
    position = jnp.arange(LEN, dtype=jnp.int32)
    valid = position[None, :] < lens_here[:, None]
    rstd = lax.rsqrt(squares / D + EPS_NORM)
    score = (rstd * product).reshape(seqs_here, LEN)
    seq_total = jnp.sum(jnp.where(valid, score, 0.0), 1)
    reward = (seq_total / lens_here.astype(jnp.float32)).reshape(pairs_here, 2)
    chosen = jnp.where(labels_here == 1, reward[:, 1], reward[:, 0])
    other = jnp.where(labels_here == 1, reward[:, 0], reward[:, 1])
    margin = chosen - other
    loss = psum_steps(jnp.sum(jax.nn.softplus(-margin)), TP_AXES)
    sig = jax.nn.sigmoid(-margin)
    first = jnp.where(labels_here == 0, -sig, sig)
    dreward = jnp.stack([first, -first], 1).reshape(-1)
    coef = jnp.where(valid, (dreward / lens_here.astype(jnp.float32))[:, None], 0.0).reshape(-1)
    cotangent = (
        coef[:, None] * (rstd[:, None] * w_vec[None, :] - (product * rstd**3 / D)[:, None] * stream)
    ).astype(jnp.bfloat16)
    cotangent_all = lax.all_gather(cotangent, TP_AXES, axis=0, tiled=True)
    contract = (((0,), (0,)), ((), ()))
    grad = lax.dot_general(gathered, cotangent_all, contract, preferred_element_type=jnp.float32)
    new_moment = 0.9 * moment + 0.1 * grad
    new_second = 0.95 * second + 0.05 * grad * grad
    m_hat = new_moment / (1.0 - 0.9**STEP)
    v_hat = new_second / (1.0 - 0.95**STEP)
    new_master = master - 0.001 * (m_hat / (jnp.sqrt(v_hat) + 1e-08) + 0.1 * master)
    return (new_master, new_moment, new_second, loss)


def solution(mesh):
    sizes = tuple(size for _, size in DP_PARTS + TP_PARTS)
    fine = Mesh(np.asarray(mesh.devices).reshape(sizes), DP_AXES + TP_AXES)
    two = P(DP_AXES, TP_AXES)
    swapped = P(TP_AXES, DP_AXES)
    return jax.shard_map(
        per_device,
        mesh=fine,
        in_specs=(
            two,
            swapped,
            swapped,
            swapped,
            swapped,
            P(DP_AXES),
            P(DP_AXES),
            P(),
            P(),
        ),
        out_specs=(swapped, swapped, swapped, P()),
        check_vma=False,
    )
```

```python
import jax
import jax.numpy as jnp
import numpy as np
from jax import lax
from jax.experimental.layout import Layout, with_layout_constraint
from jax.sharding import Mesh
from jax.sharding import PartitionSpec as P

D = 8192
LEN = 128
STEP = 100


EPS_NORM = 1e-05

DP_PARTS = (("z_hi", 2), ("y", 4), ("core", 2))
TP_PARTS = (("z_lo", 4), ("x", 4))
DP_AXES = tuple(name for name, _ in DP_PARTS)
TP_AXES = tuple(name for name, _ in TP_PARTS)


def psum_steps(value, axes):
    for axis in reversed(axes):
        value = lax.psum(value, axis)
    return value


def per_device(hidden, residual, master, moment, second, gain, head, lengths, labels):
    t_index = lax.axis_index(TP_AXES)
    block_rows = residual.shape[0]
    weights = master.astype(jnp.bfloat16)
    gathered = lax.all_gather(hidden, DP_AXES, axis=0, tiled=True)
    partial_value = jnp.dot(gathered, weights, preferred_element_type=jnp.bfloat16)
    row_start = t_index * block_rows
    own_rows = lax.dynamic_slice_in_dim(gathered, row_start, block_rows, 0)
    own = jnp.dot(own_rows, weights, preferred_element_type=jnp.float32) + residual.astype(
        jnp.float32
    )
    term = lax.dynamic_update_slice_in_dim(partial_value, own.astype(jnp.bfloat16), row_start, 0)
    w_vec = gain * head
    n_tp = term.shape[0] // block_rows
    pieces = lax.all_to_all(
        term.reshape(n_tp, block_rows, term.shape[1]), TP_AXES, 0, 0, tiled=True
    )
    stream = jnp.sum(pieces.astype(jnp.float32), 0)
    squares = jnp.sum(stream * stream, 1)
    product = jnp.sum(stream * w_vec[None, :], 1)
    squares, product = psum_steps((squares, product), DP_AXES)

    seqs_here = block_rows // LEN
    pairs_here = seqs_here // 2
    lens_flat = lengths.reshape(-1)
    lens_here = lax.dynamic_slice_in_dim(lens_flat, t_index * seqs_here, seqs_here, 0)
    labels_here = lax.dynamic_slice_in_dim(labels, t_index * pairs_here, pairs_here, 0)
    position = jnp.arange(LEN, dtype=jnp.int32)
    valid = position[None, :] < lens_here[:, None]
    rstd = lax.rsqrt(squares / D + EPS_NORM)
    score = (rstd * product).reshape(seqs_here, LEN)
    seq_total = jnp.sum(jnp.where(valid, score, 0.0), 1)
    reward = (seq_total / lens_here.astype(jnp.float32)).reshape(pairs_here, 2)
    chosen = jnp.where(labels_here == 1, reward[:, 1], reward[:, 0])
    other = jnp.where(labels_here == 1, reward[:, 0], reward[:, 1])
    margin = chosen - other
    loss = psum_steps(jnp.sum(jax.nn.softplus(-margin)), TP_AXES)
    sig = jax.nn.sigmoid(-margin)
    first = jnp.where(labels_here == 0, -sig, sig)
    dreward = jnp.stack([first, -first], 1).reshape(-1)
    coef = jnp.where(valid, (dreward / lens_here.astype(jnp.float32))[:, None], 0.0).reshape(-1)
    cotangent = (
        coef[:, None] * (rstd[:, None] * w_vec[None, :] - (product * rstd**3 / D)[:, None] * stream)
    ).astype(jnp.bfloat16)
    copies = jnp.broadcast_to(cotangent[None], (n_tp,) + cotangent.shape)
    cotangent_all = lax.all_to_all(copies, TP_AXES, 0, 0, tiled=True).reshape(-1, cotangent.shape[1])
    contract = (((0,), (0,)), ((), ()))
    grad = lax.dot_general(gathered, cotangent_all, contract, preferred_element_type=jnp.float32)
    grad = with_layout_constraint(grad, Layout(major_to_minor=(0, 1)))
    new_moment = 0.9 * moment + 0.1 * grad
    new_second = 0.95 * second + 0.05 * grad * grad
    m_hat = new_moment / (1.0 - 0.9**STEP)
    v_hat = new_second / (1.0 - 0.95**STEP)
    new_master = master - 0.001 * (m_hat / (jnp.sqrt(v_hat) + 1e-08) + 0.1 * master)
    return (new_master, new_moment, new_second, loss)


def solution(mesh):
    sizes = tuple(size for _, size in DP_PARTS + TP_PARTS)
    fine = Mesh(np.asarray(mesh.devices).reshape(sizes), DP_AXES + TP_AXES)
    two = P(DP_AXES, TP_AXES)
    swapped = P(TP_AXES, DP_AXES)
    return jax.shard_map(
        per_device,
        mesh=fine,
        in_specs=(
            two,
            swapped,
            swapped,
            swapped,
            swapped,
            P(DP_AXES),
            P(DP_AXES),
            P(),
            P(),
        ),
        out_specs=(swapped, swapped, swapped, P()),
        check_vma=False,
    )
```

```python
import jax
import jax.numpy as jnp
import numpy as np
from jax import lax
from jax.experimental.layout import Layout, with_layout_constraint
from jax.sharding import Mesh
from jax.sharding import PartitionSpec as P

D = 8192
LEN = 128
STEP = 100


EPS_NORM = 1e-05

DP_PARTS = (("z_hi", 2), ("y", 4), ("core", 2))
TP_PARTS = (("z_lo", 4), ("x", 4))
DP_AXES = tuple(name for name, _ in DP_PARTS)
TP_AXES = tuple(name for name, _ in TP_PARTS)


def psum_steps(value, axes):
    for axis in reversed(axes):
        value = lax.psum(value, axis)
    return value


def per_device(hidden, residual, master, moment, second, gain, head, lengths, labels):
    t_index = lax.axis_index(TP_AXES)
    block_rows = residual.shape[0]
    weights = master.astype(jnp.bfloat16)
    gathered = lax.all_gather(hidden, DP_AXES, axis=0, tiled=True)
    partial_value = jnp.dot(gathered, weights, preferred_element_type=jnp.bfloat16)
    row_start = t_index * block_rows
    own_rows = lax.dynamic_slice_in_dim(gathered, row_start, block_rows, 0)
    own = jnp.dot(own_rows, weights, preferred_element_type=jnp.float32) + residual.astype(
        jnp.float32
    )
    term = lax.dynamic_update_slice_in_dim(partial_value, own.astype(jnp.bfloat16), row_start, 0)
    w_vec = gain * head
    n_tp = term.shape[0] // block_rows
    pieces = lax.all_to_all(
        term.reshape(n_tp, block_rows, term.shape[1]), TP_AXES, 0, 0, tiled=True
    )
    stream = jnp.sum(pieces.astype(jnp.float32), 0)
    squares = jnp.sum(stream * stream, 1)
    product = jnp.sum(stream * w_vec[None, :], 1)
    squares, product = psum_steps((squares, product), DP_AXES)

    seqs_here = block_rows // LEN
    pairs_here = seqs_here // 2
    lens_flat = lengths.reshape(-1)
    lens_here = lax.dynamic_slice_in_dim(lens_flat, t_index * seqs_here, seqs_here, 0)
    labels_here = lax.dynamic_slice_in_dim(labels, t_index * pairs_here, pairs_here, 0)
    position = jnp.arange(LEN, dtype=jnp.int32)
    valid = position[None, :] < lens_here[:, None]
    rstd = lax.rsqrt(squares / D + EPS_NORM)
    score = (rstd * product).reshape(seqs_here, LEN)
    seq_total = jnp.sum(jnp.where(valid, score, 0.0), 1)
    reward = (seq_total / lens_here.astype(jnp.float32)).reshape(pairs_here, 2)
    chosen = jnp.where(labels_here == 1, reward[:, 1], reward[:, 0])
    other = jnp.where(labels_here == 1, reward[:, 0], reward[:, 1])
    margin = chosen - other
    loss = psum_steps(jnp.sum(jax.nn.softplus(-margin)), TP_AXES)
    sig = jax.nn.sigmoid(-margin)
    first = jnp.where(labels_here == 0, -sig, sig)
    dreward = jnp.stack([first, -first], 1).reshape(-1)
    coef = jnp.where(valid, (dreward / lens_here.astype(jnp.float32))[:, None], 0.0).reshape(-1)
    cotangent = (
        coef[:, None] * (rstd[:, None] * w_vec[None, :] - (product * rstd**3 / D)[:, None] * stream)
    ).astype(jnp.bfloat16)
    cotangent_all = lax.all_gather(cotangent, TP_AXES, axis=0, tiled=True)
    contract = (((0,), (0,)), ((), ()))
    grad = lax.dot_general(gathered, cotangent_all, contract, preferred_element_type=jnp.float32)
    grad = with_layout_constraint(grad, Layout(major_to_minor=(0, 1)))
    new_moment = 0.9 * moment + 0.1 * grad
    new_second = 0.95 * second + 0.05 * grad * grad
    m_hat = new_moment / (1.0 - 0.9**STEP)
    v_hat = new_second / (1.0 - 0.95**STEP)
    new_master = master - 0.001 * (m_hat / (jnp.sqrt(v_hat) + 1e-08) + 0.1 * master)
    return (new_master, new_moment, new_second, loss)


def solution(mesh):
    sizes = tuple(size for _, size in DP_PARTS + TP_PARTS)
    fine = Mesh(np.asarray(mesh.devices).reshape(sizes), DP_AXES + TP_AXES)
    two = P(DP_AXES, TP_AXES)
    swapped = P(TP_AXES, DP_AXES)
    return jax.shard_map(
        per_device,
        mesh=fine,
        in_specs=(
            two,
            swapped,
            swapped,
            swapped,
            swapped,
            P(DP_AXES),
            P(DP_AXES),
            P(),
            P(),
        ),
        out_specs=(swapped, swapped, swapped, P()),
        check_vma=False,
    )
```

```python
import jax
import jax.numpy as jnp
import numpy as np
from jax import lax
from jax.experimental.layout import Layout, with_layout_constraint
from jax.sharding import Mesh
from jax.sharding import PartitionSpec as P

D = 8192
LEN = 128
STEP = 100


EPS_NORM = 1e-05

DP_PARTS = (("z_hi", 2), ("y", 4), ("core", 2))
TP_PARTS = (("z_lo", 4), ("x", 4))
DP_AXES = tuple(name for name, _ in DP_PARTS)
TP_AXES = tuple(name for name, _ in TP_PARTS)


def psum_steps(value, axes):
    for axis in reversed(axes):
        value = lax.psum(value, axis)
    return value


def per_device(hidden, residual, master, moment, second, gain, head, lengths, labels):
    t_index = lax.axis_index(TP_AXES)
    block_rows = residual.shape[0]
    weights = master.astype(jnp.bfloat16)
    gathered = lax.all_gather(hidden, DP_AXES, axis=0, tiled=True)
    partial_value = jnp.dot(gathered, weights, preferred_element_type=jnp.bfloat16)
    row_start = t_index * block_rows
    own_rows = lax.dynamic_slice_in_dim(gathered, row_start, block_rows, 0)
    own = jnp.dot(own_rows, weights, preferred_element_type=jnp.float32) + residual.astype(
        jnp.float32
    )
    term = lax.dynamic_update_slice_in_dim(partial_value, own.astype(jnp.bfloat16), row_start, 0)
    w_vec = gain * head
    n_tp = term.shape[0] // block_rows
    pieces = lax.all_to_all(
        term.reshape(n_tp, block_rows, term.shape[1]), TP_AXES, 0, 0, tiled=True
    )
    stream = jnp.sum(pieces.astype(jnp.float32), 0)
    squares = jnp.sum(stream * stream, 1)
    product = jnp.sum(stream * w_vec[None, :], 1)
    squares, product = psum_steps((squares, product), DP_AXES)

    seqs_here = block_rows // LEN
    pairs_here = seqs_here // 2
    lens_flat = lengths.reshape(-1)
    lens_here = lax.dynamic_slice_in_dim(lens_flat, t_index * seqs_here, seqs_here, 0)
    labels_here = lax.dynamic_slice_in_dim(labels, t_index * pairs_here, pairs_here, 0)
    position = jnp.arange(LEN, dtype=jnp.int32)
    valid = position[None, :] < lens_here[:, None]
    rstd = lax.rsqrt(squares / D + EPS_NORM)
    score = (rstd * product).reshape(seqs_here, LEN)
    seq_total = jnp.sum(jnp.where(valid, score, 0.0), 1)
    reward = (seq_total / lens_here.astype(jnp.float32)).reshape(pairs_here, 2)
    chosen = jnp.where(labels_here == 1, reward[:, 1], reward[:, 0])
    other = jnp.where(labels_here == 1, reward[:, 0], reward[:, 1])
    margin = chosen - other
    loss_here = jnp.sum(jax.nn.softplus(-margin))
    sig = jax.nn.sigmoid(-margin)
    first = jnp.where(labels_here == 0, -sig, sig)
    dreward = jnp.stack([first, -first], 1).reshape(-1)
    coef = jnp.where(valid, (dreward / lens_here.astype(jnp.float32))[:, None], 0.0).reshape(-1)
    cotangent = (
        coef[:, None] * (rstd[:, None] * w_vec[None, :] - (product * rstd**3 / D)[:, None] * stream)
    ).astype(jnp.bfloat16)
    high = loss_here.astype(jnp.bfloat16)
    low = (loss_here - high.astype(jnp.float32)).astype(jnp.bfloat16)
    spare = jnp.zeros((16, cotangent.shape[1]), jnp.bfloat16)
    spare = spare.at[0, 0].set(high).at[0, 1].set(low)
    payload = jnp.concatenate([cotangent, spare], 0)
    payload_all = lax.all_gather(payload, TP_AXES, axis=0, tiled=False)
    cotangent_all = payload_all[:, :block_rows].reshape(-1, cotangent.shape[1])
    loss_terms = payload_all[:, block_rows, :2].astype(jnp.float32)
    loss = jnp.sum(loss_terms[:, 0] + loss_terms[:, 1])
    contract = (((0,), (0,)), ((), ()))
    grad = lax.dot_general(gathered, cotangent_all, contract, preferred_element_type=jnp.float32)
    grad = with_layout_constraint(grad, Layout(major_to_minor=(0, 1)))
    new_moment = 0.9 * moment + 0.1 * grad
    new_second = 0.95 * second + 0.05 * grad * grad
    m_hat = new_moment / (1.0 - 0.9**STEP)
    v_hat = new_second / (1.0 - 0.95**STEP)
    new_master = master - 0.001 * (m_hat / (jnp.sqrt(v_hat) + 1e-08) + 0.1 * master)
    return (new_master, new_moment, new_second, loss)


def solution(mesh):
    sizes = tuple(size for _, size in DP_PARTS + TP_PARTS)
    fine = Mesh(np.asarray(mesh.devices).reshape(sizes), DP_AXES + TP_AXES)
    two = P(DP_AXES, TP_AXES)
    swapped = P(TP_AXES, DP_AXES)
    return jax.shard_map(
        per_device,
        mesh=fine,
        in_specs=(
            two,
            swapped,
            swapped,
            swapped,
            swapped,
            P(DP_AXES),
            P(DP_AXES),
            P(),
            P(),
        ),
        out_specs=(swapped, swapped, swapped, P()),
        check_vma=False,
    )
```

```python
import jax
import jax.numpy as jnp
import numpy as np
from jax import lax
from jax.experimental.layout import Layout, with_layout_constraint
from jax.sharding import Mesh
from jax.sharding import PartitionSpec as P

D = 8192
LEN = 128
STEP = 100


EPS_NORM = 1e-05

DP_PARTS = (("z_hi", 2), ("y", 4), ("core", 2))
TP_PARTS = (("z_lo", 4), ("x", 4))
DP_AXES = tuple(name for name, _ in DP_PARTS)
TP_AXES = tuple(name for name, _ in TP_PARTS)


def psum_steps(value, axes):
    for axis in reversed(axes):
        value = lax.psum(value, axis)
    return value


def per_device(hidden, residual, master, moment, second, gain, head, lengths, labels):
    t_index = lax.axis_index(TP_AXES)
    block_rows = residual.shape[0]
    seqs_here = block_rows // LEN
    weights = master.astype(jnp.bfloat16)
    gathered = []
    stream_parts = []
    for k in range(seqs_here):
        rows = slice(k * LEN, (k + 1) * LEN)
        part_in = lax.all_gather(hidden[rows], DP_AXES, axis=0, tiled=False)
        gathered.append(part_in)
        n_blocks = part_in.shape[0]
        flat = part_in.reshape(-1, part_in.shape[-1])
        partial_value = jnp.dot(flat, weights, preferred_element_type=jnp.bfloat16)
        partial_value = partial_value.reshape(n_blocks, LEN, -1)
        own_rows = lax.dynamic_index_in_dim(part_in, t_index, 0, keepdims=False)
        own = jnp.dot(own_rows, weights, preferred_element_type=jnp.float32) + residual[
            rows
        ].astype(jnp.float32)
        term = lax.dynamic_update_index_in_dim(partial_value, own.astype(jnp.bfloat16), t_index, 0)
        pieces = lax.all_to_all(term, TP_AXES, 0, 0, tiled=True)
        stream_parts.append(jnp.sum(pieces.astype(jnp.float32), 0))
    stream = jnp.concatenate(stream_parts, 0)
    w_vec = gain * head
    squares = jnp.sum(stream * stream, 1)
    product = jnp.sum(stream * w_vec[None, :], 1)
    squares, product = psum_steps((squares, product), DP_AXES)

    pairs_here = seqs_here // 2
    lens_flat = lengths.reshape(-1)
    lens_here = lax.dynamic_slice_in_dim(lens_flat, t_index * seqs_here, seqs_here, 0)
    labels_here = lax.dynamic_slice_in_dim(labels, t_index * pairs_here, pairs_here, 0)
    position = jnp.arange(LEN, dtype=jnp.int32)
    valid = position[None, :] < lens_here[:, None]
    rstd = lax.rsqrt(squares / D + EPS_NORM)
    score = (rstd * product).reshape(seqs_here, LEN)
    seq_total = jnp.sum(jnp.where(valid, score, 0.0), 1)
    reward = (seq_total / lens_here.astype(jnp.float32)).reshape(pairs_here, 2)
    chosen = jnp.where(labels_here == 1, reward[:, 1], reward[:, 0])
    other = jnp.where(labels_here == 1, reward[:, 0], reward[:, 1])
    margin = chosen - other
    loss = psum_steps(jnp.sum(jax.nn.softplus(-margin)), TP_AXES)
    sig = jax.nn.sigmoid(-margin)
    first = jnp.where(labels_here == 0, -sig, sig)
    dreward = jnp.stack([first, -first], 1).reshape(-1)
    coef = jnp.where(valid, (dreward / lens_here.astype(jnp.float32))[:, None], 0.0).reshape(-1)
    cotangent = (
        coef[:, None] * (rstd[:, None] * w_vec[None, :] - (product * rstd**3 / D)[:, None] * stream)
    ).astype(jnp.bfloat16)
    cotangent_all = lax.all_gather(
        cotangent.reshape(seqs_here, LEN, -1), TP_AXES, axis=1, tiled=False
    )
    contract = (((0,), (0,)), ((), ()))
    grad = sum(
        lax.dot_general(
            part_in.reshape(-1, part_in.shape[-1]),
            cotangent_all[k].reshape(-1, cotangent_all.shape[-1]),
            contract,
            preferred_element_type=jnp.float32,
        )
        for k, part_in in enumerate(gathered)
    )
    grad = with_layout_constraint(grad, Layout(major_to_minor=(0, 1)))
    new_moment = 0.9 * moment + 0.1 * grad
    new_second = 0.95 * second + 0.05 * grad * grad
    m_hat = new_moment / (1.0 - 0.9**STEP)
    v_hat = new_second / (1.0 - 0.95**STEP)
    new_master = master - 0.001 * (m_hat / (jnp.sqrt(v_hat) + 1e-08) + 0.1 * master)
    return (new_master, new_moment, new_second, loss)


def solution(mesh):
    sizes = tuple(size for _, size in DP_PARTS + TP_PARTS)
    fine = Mesh(np.asarray(mesh.devices).reshape(sizes), DP_AXES + TP_AXES)
    two = P(DP_AXES, TP_AXES)
    swapped = P(TP_AXES, DP_AXES)
    return jax.shard_map(
        per_device,
        mesh=fine,
        in_specs=(
            two,
            swapped,
            swapped,
            swapped,
            swapped,
            P(DP_AXES),
            P(DP_AXES),
            P(),
            P(),
        ),
        out_specs=(swapped, swapped, swapped, P()),
        check_vma=False,
    )
```

```python
import jax
import jax.numpy as jnp
import numpy as np
from jax import lax
from jax.experimental.layout import Layout, with_layout_constraint
from jax.sharding import Mesh
from jax.sharding import PartitionSpec as P

D = 8192
LEN = 128
STEP = 100


EPS_NORM = 1e-05

DP_PARTS = (("z_hi", 2), ("y", 4), ("core", 2))
TP_PARTS = (("z_lo", 4), ("x", 4))
DP_AXES = tuple(name for name, _ in DP_PARTS)
TP_AXES = tuple(name for name, _ in TP_PARTS)


def psum_steps(value, axes):
    for axis in reversed(axes):
        value = lax.psum(value, axis)
    return value


def per_device(hidden, residual, master, moment, second, gain, head, lengths, labels):
    t_index = lax.axis_index(TP_AXES)
    block_rows = residual.shape[0]
    weights = master.astype(jnp.bfloat16)
    gathered = lax.all_gather(hidden, DP_AXES, axis=0, tiled=True)
    partial_value = jnp.dot(gathered, weights, preferred_element_type=jnp.float32)
    row_start = t_index * block_rows
    own = lax.dynamic_slice_in_dim(partial_value, row_start, block_rows, 0) + residual.astype(
        jnp.float32
    )
    term = lax.dynamic_update_slice_in_dim(partial_value, own, row_start, 0)
    w_vec = gain * head
    stream = lax.psum_scatter(
        term.astype(jnp.bfloat16), TP_AXES, scatter_dimension=0, tiled=True
    ).astype(jnp.float32)
    squares = jnp.sum(stream * stream, 1)
    product = jnp.sum(stream * w_vec[None, :], 1)
    squares, product = psum_steps((squares, product), DP_AXES)

    seqs_here = block_rows // LEN
    pairs_here = seqs_here // 2
    lens_flat = lengths.reshape(-1)
    lens_here = lax.dynamic_slice_in_dim(lens_flat, t_index * seqs_here, seqs_here, 0)
    labels_here = lax.dynamic_slice_in_dim(labels, t_index * pairs_here, pairs_here, 0)
    position = jnp.arange(LEN, dtype=jnp.int32)
    valid = position[None, :] < lens_here[:, None]
    rstd = lax.rsqrt(squares / D + EPS_NORM)
    score = (rstd * product).reshape(seqs_here, LEN)
    seq_total = jnp.sum(jnp.where(valid, score, 0.0), 1)
    reward = (seq_total / lens_here.astype(jnp.float32)).reshape(pairs_here, 2)
    chosen = jnp.where(labels_here == 1, reward[:, 1], reward[:, 0])
    other = jnp.where(labels_here == 1, reward[:, 0], reward[:, 1])
    margin = chosen - other
    loss = psum_steps(jnp.sum(jax.nn.softplus(-margin)), TP_AXES)
    sig = jax.nn.sigmoid(-margin)
    first = jnp.where(labels_here == 0, -sig, sig)
    dreward = jnp.stack([first, -first], 1).reshape(-1)
    coef = jnp.where(valid, (dreward / lens_here.astype(jnp.float32))[:, None], 0.0).reshape(-1)
    cotangent = (
        coef[:, None] * (rstd[:, None] * w_vec[None, :] - (product * rstd**3 / D)[:, None] * stream)
    ).astype(jnp.bfloat16)
    cotangent_all = lax.all_gather(cotangent, TP_AXES, axis=0, tiled=True)
    contract = (((0,), (0,)), ((), ()))
    grad = lax.dot_general(gathered, cotangent_all, contract, preferred_element_type=jnp.float32)
    grad = with_layout_constraint(grad, Layout(major_to_minor=(0, 1)))
    new_moment = 0.9 * moment + 0.1 * grad
    new_second = 0.95 * second + 0.05 * grad * grad
    m_hat = new_moment / (1.0 - 0.9**STEP)
    v_hat = new_second / (1.0 - 0.95**STEP)
    new_master = master - 0.001 * (m_hat / (jnp.sqrt(v_hat) + 1e-08) + 0.1 * master)
    return (new_master, new_moment, new_second, loss)


def solution(mesh):
    sizes = tuple(size for _, size in DP_PARTS + TP_PARTS)
    fine = Mesh(np.asarray(mesh.devices).reshape(sizes), DP_AXES + TP_AXES)
    two = P(DP_AXES, TP_AXES)
    swapped = P(TP_AXES, DP_AXES)
    return jax.shard_map(
        per_device,
        mesh=fine,
        in_specs=(
            two,
            swapped,
            swapped,
            swapped,
            swapped,
            P(DP_AXES),
            P(DP_AXES),
            P(),
            P(),
        ),
        out_specs=(swapped, swapped, swapped, P()),
        check_vma=False,
    )
```

```python
import jax
import jax.numpy as jnp
import numpy as np
from jax import lax
from jax.experimental.layout import Layout, with_layout_constraint
from jax.sharding import Mesh
from jax.sharding import PartitionSpec as P

D = 8192
LEN = 128
STEP = 100


EPS_NORM = 1e-05

DP_PARTS = (("z_hi", 2), ("y", 4), ("core", 2))
TP_PARTS = (("z_lo", 4), ("x", 4))
DP_AXES = tuple(name for name, _ in DP_PARTS)
TP_AXES = tuple(name for name, _ in TP_PARTS)


def exchange_sum(value, parts):
    for name, size in reversed(parts):
        bit = 1
        while bit < size:
            pairs = [(i, i ^ bit) for i in range(size)]
            value = value + lax.ppermute(value, name, pairs)
            bit *= 2
    return value


def psum_steps(value, axes):
    for axis in reversed(axes):
        value = lax.psum(value, axis)
    return value


def per_device(hidden, residual, master, moment, second, gain, head, lengths, labels):
    t_index = lax.axis_index(TP_AXES)
    block_rows = residual.shape[0]
    weights = master.astype(jnp.bfloat16)
    gathered = lax.all_gather(hidden, DP_AXES, axis=0, tiled=True)
    partial_value = jnp.dot(gathered, weights, preferred_element_type=jnp.float32)
    row_start = t_index * block_rows
    own = lax.dynamic_slice_in_dim(partial_value, row_start, block_rows, 0) + residual.astype(
        jnp.float32
    )
    term = lax.dynamic_update_slice_in_dim(partial_value, own, row_start, 0)
    w_vec = gain * head
    stream = lax.psum_scatter(
        term.astype(jnp.bfloat16), TP_AXES, scatter_dimension=0, tiled=True
    ).astype(jnp.float32)
    squares = jnp.sum(stream * stream, 1)
    product = jnp.sum(stream * w_vec[None, :], 1)
    squares, product = exchange_sum(jnp.stack([squares, product]), DP_PARTS)

    seqs_here = block_rows // LEN
    pairs_here = seqs_here // 2
    lens_flat = lengths.reshape(-1)
    lens_here = lax.dynamic_slice_in_dim(lens_flat, t_index * seqs_here, seqs_here, 0)
    labels_here = lax.dynamic_slice_in_dim(labels, t_index * pairs_here, pairs_here, 0)
    position = jnp.arange(LEN, dtype=jnp.int32)
    valid = position[None, :] < lens_here[:, None]
    rstd = lax.rsqrt(squares / D + EPS_NORM)
    score = (rstd * product).reshape(seqs_here, LEN)
    seq_total = jnp.sum(jnp.where(valid, score, 0.0), 1)
    reward = (seq_total / lens_here.astype(jnp.float32)).reshape(pairs_here, 2)
    chosen = jnp.where(labels_here == 1, reward[:, 1], reward[:, 0])
    other = jnp.where(labels_here == 1, reward[:, 0], reward[:, 1])
    margin = chosen - other
    loss = psum_steps(jnp.sum(jax.nn.softplus(-margin)), TP_AXES)
    sig = jax.nn.sigmoid(-margin)
    first = jnp.where(labels_here == 0, -sig, sig)
    dreward = jnp.stack([first, -first], 1).reshape(-1)
    coef = jnp.where(valid, (dreward / lens_here.astype(jnp.float32))[:, None], 0.0).reshape(-1)
    cotangent = (
        coef[:, None] * (rstd[:, None] * w_vec[None, :] - (product * rstd**3 / D)[:, None] * stream)
    ).astype(jnp.bfloat16)
    cotangent_all = lax.all_gather(cotangent, TP_AXES, axis=0, tiled=True)
    contract = (((0,), (0,)), ((), ()))
    grad = lax.dot_general(gathered, cotangent_all, contract, preferred_element_type=jnp.float32)
    grad = with_layout_constraint(grad, Layout(major_to_minor=(0, 1)))
    new_moment = 0.9 * moment + 0.1 * grad
    new_second = 0.95 * second + 0.05 * grad * grad
    m_hat = new_moment / (1.0 - 0.9**STEP)
    v_hat = new_second / (1.0 - 0.95**STEP)
    new_master = master - 0.001 * (m_hat / (jnp.sqrt(v_hat) + 1e-08) + 0.1 * master)
    return (new_master, new_moment, new_second, loss)


def solution(mesh):
    sizes = tuple(size for _, size in DP_PARTS + TP_PARTS)
    fine = Mesh(np.asarray(mesh.devices).reshape(sizes), DP_AXES + TP_AXES)
    two = P(DP_AXES, TP_AXES)
    swapped = P(TP_AXES, DP_AXES)
    return jax.shard_map(
        per_device,
        mesh=fine,
        in_specs=(
            two,
            swapped,
            swapped,
            swapped,
            swapped,
            P(DP_AXES),
            P(DP_AXES),
            P(),
            P(),
        ),
        out_specs=(swapped, swapped, swapped, P()),
        check_vma=False,
    )
```

```python
import jax
import jax.numpy as jnp
import numpy as np
from jax import lax
from jax.experimental.layout import Layout, with_layout_constraint
from jax.sharding import Mesh
from jax.sharding import PartitionSpec as P

D = 8192
LEN = 128
STEP = 100


EPS_NORM = 1e-05

DP_PARTS = (("z_hi", 2), ("y", 4), ("core", 2))
TP_PARTS = (("z_lo", 4), ("x", 4))
DP_AXES = tuple(name for name, _ in DP_PARTS)
TP_AXES = tuple(name for name, _ in TP_PARTS)


def exchange_sum(value, parts):
    (core_name, core_size) = parts[-1]
    bit = 1
    while bit < core_size:
        value = value + lax.ppermute(value, core_name, [(i, i ^ bit) for i in range(core_size)])
        bit *= 2
    names = tuple(name for name, _ in parts[:-1])
    n = 1
    for _, size in parts[:-1]:
        n *= size
    me = lax.axis_index(names)
    received = [value] + [
        lax.ppermute(value, names, [(i, (i + shift) % n) for i in range(n)]) for shift in range(1, n)
    ]
    in_order = jnp.stack(received)[(me - jnp.arange(n)) % n]
    total = in_order[0]
    for k in range(1, n):
        total = total + in_order[k]
    return total


def psum_steps(value, axes):
    for axis in reversed(axes):
        value = lax.psum(value, axis)
    return value


def per_device(hidden, residual, master, moment, second, gain, head, lengths, labels):
    t_index = lax.axis_index(TP_AXES)
    block_rows = residual.shape[0]
    weights = master.astype(jnp.bfloat16)
    gathered = lax.all_gather(hidden, DP_AXES, axis=0, tiled=True)
    partial_value = jnp.dot(gathered, weights, preferred_element_type=jnp.float32)
    row_start = t_index * block_rows
    own = lax.dynamic_slice_in_dim(partial_value, row_start, block_rows, 0) + residual.astype(
        jnp.float32
    )
    term = lax.dynamic_update_slice_in_dim(partial_value, own, row_start, 0)
    w_vec = gain * head
    stream = lax.psum_scatter(
        term.astype(jnp.bfloat16), TP_AXES, scatter_dimension=0, tiled=True
    ).astype(jnp.float32)
    squares = jnp.sum(stream * stream, 1)
    product = jnp.sum(stream * w_vec[None, :], 1)
    squares, product = exchange_sum(jnp.stack([squares, product]), DP_PARTS)

    seqs_here = block_rows // LEN
    pairs_here = seqs_here // 2
    lens_flat = lengths.reshape(-1)
    lens_here = lax.dynamic_slice_in_dim(lens_flat, t_index * seqs_here, seqs_here, 0)
    labels_here = lax.dynamic_slice_in_dim(labels, t_index * pairs_here, pairs_here, 0)
    position = jnp.arange(LEN, dtype=jnp.int32)
    valid = position[None, :] < lens_here[:, None]
    rstd = lax.rsqrt(squares / D + EPS_NORM)
    score = (rstd * product).reshape(seqs_here, LEN)
    seq_total = jnp.sum(jnp.where(valid, score, 0.0), 1)
    reward = (seq_total / lens_here.astype(jnp.float32)).reshape(pairs_here, 2)
    chosen = jnp.where(labels_here == 1, reward[:, 1], reward[:, 0])
    other = jnp.where(labels_here == 1, reward[:, 0], reward[:, 1])
    margin = chosen - other
    loss = psum_steps(jnp.sum(jax.nn.softplus(-margin)), TP_AXES)
    sig = jax.nn.sigmoid(-margin)
    first = jnp.where(labels_here == 0, -sig, sig)
    dreward = jnp.stack([first, -first], 1).reshape(-1)
    coef = jnp.where(valid, (dreward / lens_here.astype(jnp.float32))[:, None], 0.0).reshape(-1)
    cotangent = (
        coef[:, None] * (rstd[:, None] * w_vec[None, :] - (product * rstd**3 / D)[:, None] * stream)
    ).astype(jnp.bfloat16)
    cotangent_all = lax.all_gather(cotangent, TP_AXES, axis=0, tiled=True)
    contract = (((0,), (0,)), ((), ()))
    grad = lax.dot_general(gathered, cotangent_all, contract, preferred_element_type=jnp.float32)
    grad = with_layout_constraint(grad, Layout(major_to_minor=(0, 1)))
    new_moment = 0.9 * moment + 0.1 * grad
    new_second = 0.95 * second + 0.05 * grad * grad
    m_hat = new_moment / (1.0 - 0.9**STEP)
    v_hat = new_second / (1.0 - 0.95**STEP)
    new_master = master - 0.001 * (m_hat / (jnp.sqrt(v_hat) + 1e-08) + 0.1 * master)
    return (new_master, new_moment, new_second, loss)


def solution(mesh):
    sizes = tuple(size for _, size in DP_PARTS + TP_PARTS)
    fine = Mesh(np.asarray(mesh.devices).reshape(sizes), DP_AXES + TP_AXES)
    two = P(DP_AXES, TP_AXES)
    swapped = P(TP_AXES, DP_AXES)
    return jax.shard_map(
        per_device,
        mesh=fine,
        in_specs=(
            two,
            swapped,
            swapped,
            swapped,
            swapped,
            P(DP_AXES),
            P(DP_AXES),
            P(),
            P(),
        ),
        out_specs=(swapped, swapped, swapped, P()),
        check_vma=False,
    )
```

```python
import jax
import jax.numpy as jnp
import numpy as np
from jax import lax
from jax.experimental.layout import Layout, with_layout_constraint
from jax.sharding import Mesh
from jax.sharding import PartitionSpec as P

D = 8192
LEN = 128
STEP = 100


EPS_NORM = 1e-05

DP_PARTS = (("z_hi", 2), ("y", 4), ("core", 2))
TP_PARTS = (("z_lo", 4), ("x", 4))
DP_AXES = tuple(name for name, _ in DP_PARTS)
TP_AXES = tuple(name for name, _ in TP_PARTS)


def exchange_sum(value, parts):
    for name, size in reversed(parts):
        bit = 1
        while bit < size:
            pairs = [(i, i ^ bit) for i in range(size)]
            value = value + lax.ppermute(value, name, pairs)
            bit *= 2
    return value


def psum_steps(value, axes):
    for axis in reversed(axes):
        value = lax.psum(value, axis)
    return value


def per_device(hidden, residual, master, moment, second, gain, head, lengths, labels):
    t_index = lax.axis_index(TP_AXES)
    block_rows = residual.shape[0]
    weights = master.astype(jnp.bfloat16)
    gathered = lax.all_gather(hidden, DP_AXES, axis=0, tiled=True)
    partial_value = jnp.dot(gathered, weights, preferred_element_type=jnp.float32)
    row_start = t_index * block_rows
    own = lax.dynamic_slice_in_dim(partial_value, row_start, block_rows, 0) + residual.astype(
        jnp.float32
    )
    term = lax.dynamic_update_slice_in_dim(partial_value, own, row_start, 0).astype(jnp.bfloat16)
    w_vec = gain * head
    n_tp = term.shape[0] // block_rows
    pieces = lax.all_to_all(
        term.reshape(n_tp, block_rows, term.shape[1]), TP_AXES, 0, 0, tiled=True
    )
    stream = jnp.sum(pieces.astype(jnp.float32), 0)
    squares = jnp.sum(stream * stream, 1)
    product = jnp.sum(stream * w_vec[None, :], 1)
    squares, product = exchange_sum(jnp.stack([squares, product]), DP_PARTS)

    seqs_here = block_rows // LEN
    pairs_here = seqs_here // 2
    lens_flat = lengths.reshape(-1)
    lens_here = lax.dynamic_slice_in_dim(lens_flat, t_index * seqs_here, seqs_here, 0)
    labels_here = lax.dynamic_slice_in_dim(labels, t_index * pairs_here, pairs_here, 0)
    position = jnp.arange(LEN, dtype=jnp.int32)
    valid = position[None, :] < lens_here[:, None]
    rstd = lax.rsqrt(squares / D + EPS_NORM)
    score = (rstd * product).reshape(seqs_here, LEN)
    seq_total = jnp.sum(jnp.where(valid, score, 0.0), 1)
    reward = (seq_total / lens_here.astype(jnp.float32)).reshape(pairs_here, 2)
    chosen = jnp.where(labels_here == 1, reward[:, 1], reward[:, 0])
    other = jnp.where(labels_here == 1, reward[:, 0], reward[:, 1])
    margin = chosen - other
    loss_here = jnp.sum(jax.nn.softplus(-margin))
    sig = jax.nn.sigmoid(-margin)
    first = jnp.where(labels_here == 0, -sig, sig)
    dreward = jnp.stack([first, -first], 1).reshape(-1)
    coef = jnp.where(valid, (dreward / lens_here.astype(jnp.float32))[:, None], 0.0).reshape(-1)
    cotangent = (
        coef[:, None] * (rstd[:, None] * w_vec[None, :] - (product * rstd**3 / D)[:, None] * stream)
    ).astype(jnp.bfloat16)
    high = loss_here.astype(jnp.bfloat16)
    low = (loss_here - high.astype(jnp.float32)).astype(jnp.bfloat16)
    spare = jnp.zeros((16, cotangent.shape[1]), jnp.bfloat16)
    spare = spare.at[0, 0].set(high).at[0, 1].set(low)
    payload = jnp.concatenate([cotangent, spare], 0)
    copies = jnp.broadcast_to(payload[None], (n_tp,) + payload.shape)
    payload_all = lax.all_to_all(copies, TP_AXES, 0, 0, tiled=True)
    cotangent_all = payload_all[:, :block_rows].reshape(-1, cotangent.shape[1])
    loss_terms = payload_all[:, block_rows, :2].astype(jnp.float32)
    loss = jnp.sum(loss_terms[:, 0] + loss_terms[:, 1])
    contract = (((0,), (0,)), ((), ()))
    grad = lax.dot_general(gathered, cotangent_all, contract, preferred_element_type=jnp.float32)
    grad = with_layout_constraint(grad, Layout(major_to_minor=(0, 1)))
    new_moment = 0.9 * moment + 0.1 * grad
    new_second = 0.95 * second + 0.05 * grad * grad
    m_hat = new_moment / (1.0 - 0.9**STEP)
    v_hat = new_second / (1.0 - 0.95**STEP)
    new_master = master - 0.001 * (m_hat / (jnp.sqrt(v_hat) + 1e-08) + 0.1 * master)
    return (new_master, new_moment, new_second, loss)


def solution(mesh):
    sizes = tuple(size for _, size in DP_PARTS + TP_PARTS)
    fine = Mesh(np.asarray(mesh.devices).reshape(sizes), DP_AXES + TP_AXES)
    two = P(DP_AXES, TP_AXES)
    swapped = P(TP_AXES, DP_AXES)
    return jax.shard_map(
        per_device,
        mesh=fine,
        in_specs=(
            two,
            swapped,
            swapped,
            swapped,
            swapped,
            P(DP_AXES),
            P(DP_AXES),
            P(),
            P(),
        ),
        out_specs=(swapped, swapped, swapped, P()),
        check_vma=False,
    )
```

```python
import jax
import jax.numpy as jnp
import numpy as np
from jax import lax
from jax.experimental.layout import Layout, with_layout_constraint
from jax.sharding import Mesh
from jax.sharding import PartitionSpec as P

D = 8192
LEN = 128
STEP = 100


EPS_NORM = 1e-05

DP_PARTS = (("z_hi", 2), ("y", 4), ("core", 2))
TP_PARTS = (("z_lo", 4), ("x", 4))
DP_AXES = tuple(name for name, _ in DP_PARTS)
TP_AXES = tuple(name for name, _ in TP_PARTS)


def exchange_sum(value, parts):
    for name, size in reversed(parts):
        bit = 1
        while bit < size:
            pairs = [(i, i ^ bit) for i in range(size)]
            value = value + lax.ppermute(value, name, pairs)
            bit *= 2
    return value


def psum_steps(value, axes):
    for axis in reversed(axes):
        value = lax.psum(value, axis)
    return value


def per_device(hidden, residual, master, moment, second, gain, head, lengths, labels):
    t_index = lax.axis_index(TP_AXES)
    block_rows = residual.shape[0]
    weights = master.astype(jnp.bfloat16)
    gathered = lax.all_gather(hidden, DP_AXES, axis=0, tiled=True)
    partial_value = jnp.dot(gathered, weights, preferred_element_type=jnp.float32)
    n_tp = partial_value.shape[0] // block_rows
    mine = (jnp.arange(n_tp, dtype=jnp.int32) == t_index)[:, None, None]
    resid_rows = jnp.where(mine, residual.astype(jnp.float32)[None], 0.0)
    term = partial_value + resid_rows.reshape(partial_value.shape)
    w_vec = gain * head
    stream = lax.psum_scatter(
        term.astype(jnp.bfloat16), TP_AXES, scatter_dimension=0, tiled=True
    ).astype(jnp.float32)
    squares = jnp.sum(stream * stream, 1)
    product = jnp.sum(stream * w_vec[None, :], 1)
    squares, product = exchange_sum(jnp.stack([squares, product]), DP_PARTS)

    seqs_here = block_rows // LEN
    pairs_here = seqs_here // 2
    lens_flat = lengths.reshape(-1)
    lens_here = lax.dynamic_slice_in_dim(lens_flat, t_index * seqs_here, seqs_here, 0)
    labels_here = lax.dynamic_slice_in_dim(labels, t_index * pairs_here, pairs_here, 0)
    position = jnp.arange(LEN, dtype=jnp.int32)
    valid = position[None, :] < lens_here[:, None]
    rstd = lax.rsqrt(squares / D + EPS_NORM)
    score = (rstd * product).reshape(seqs_here, LEN)
    seq_total = jnp.sum(jnp.where(valid, score, 0.0), 1)
    reward = (seq_total / lens_here.astype(jnp.float32)).reshape(pairs_here, 2)
    chosen = jnp.where(labels_here == 1, reward[:, 1], reward[:, 0])
    other = jnp.where(labels_here == 1, reward[:, 0], reward[:, 1])
    margin = chosen - other
    loss = psum_steps(jnp.sum(jax.nn.softplus(-margin)), TP_AXES)
    sig = jax.nn.sigmoid(-margin)
    first = jnp.where(labels_here == 0, -sig, sig)
    dreward = jnp.stack([first, -first], 1).reshape(-1)
    coef = jnp.where(valid, (dreward / lens_here.astype(jnp.float32))[:, None], 0.0).reshape(-1)
    cotangent = (
        coef[:, None] * (rstd[:, None] * w_vec[None, :] - (product * rstd**3 / D)[:, None] * stream)
    ).astype(jnp.bfloat16)
    cotangent_all = lax.all_gather(cotangent, TP_AXES, axis=0, tiled=True)
    contract = (((0,), (0,)), ((), ()))
    grad = lax.dot_general(gathered, cotangent_all, contract, preferred_element_type=jnp.float32)
    grad = with_layout_constraint(grad, Layout(major_to_minor=(0, 1)))
    new_moment = 0.9 * moment + 0.1 * grad
    new_second = 0.95 * second + 0.05 * grad * grad
    m_hat = new_moment / (1.0 - 0.9**STEP)
    v_hat = new_second / (1.0 - 0.95**STEP)
    new_master = master - 0.001 * (m_hat / (jnp.sqrt(v_hat) + 1e-08) + 0.1 * master)
    return (new_master, new_moment, new_second, loss)


def solution(mesh):
    sizes = tuple(size for _, size in DP_PARTS + TP_PARTS)
    fine = Mesh(np.asarray(mesh.devices).reshape(sizes), DP_AXES + TP_AXES)
    two = P(DP_AXES, TP_AXES)
    swapped = P(TP_AXES, DP_AXES)
    return jax.shard_map(
        per_device,
        mesh=fine,
        in_specs=(
            two,
            swapped,
            swapped,
            swapped,
            swapped,
            P(DP_AXES),
            P(DP_AXES),
            P(),
            P(),
        ),
        out_specs=(swapped, swapped, swapped, P()),
        check_vma=False,
    )
```

```python
import jax
import jax.numpy as jnp
import numpy as np
from jax import lax
from jax.experimental import pallas as pl
from jax.experimental.layout import Layout, with_layout_constraint
from jax.sharding import Mesh
from jax.sharding import PartitionSpec as P

D = 8192
LEN = 128
STEP = 100


EPS_NORM = 1e-05

DP_PARTS = (("z_hi", 2), ("y", 4), ("core", 2))
TP_PARTS = (("z_lo", 4), ("x", 4))
DP_AXES = tuple(name for name, _ in DP_PARTS)
TP_AXES = tuple(name for name, _ in TP_PARTS)


def exchange_sum(value, parts):
    for name, size in reversed(parts):
        bit = 1
        while bit < size:
            pairs = [(i, i ^ bit) for i in range(size)]
            value = value + lax.ppermute(value, name, pairs)
            bit *= 2
    return value


def adamw_kernel(hid_ref, cot_ref, master_ref, moment_ref, second_ref, out_master, out_moment, out_second):
    contract = (((0,), (0,)), ((), ()))
    grad = lax.dot_general(hid_ref[...], cot_ref[...], contract, preferred_element_type=jnp.float32)
    master = master_ref[...]
    new_moment = 0.9 * moment_ref[...] + 0.1 * grad
    new_second = 0.95 * second_ref[...] + 0.05 * grad * grad
    m_hat = new_moment / (1.0 - 0.9**STEP)
    v_hat = new_second / (1.0 - 0.95**STEP)
    out_master[...] = master - 0.001 * (m_hat / (jnp.sqrt(v_hat) + 1e-08) + 0.1 * master)
    out_moment[...] = new_moment
    out_second[...] = new_second


def grad_step(gathered, cotangent_all, master, moment, second, tile=128):
    tokens, units = gathered.shape
    width = cotangent_all.shape[1]
    state = pl.BlockSpec((tile, width), lambda i: (i, 0))
    shape = jax.ShapeDtypeStruct((units, width), jnp.float32)
    cost = pl.CostEstimate(
        flops=2 * tokens * units * width,
        transcendentals=units * width,
        bytes_accessed=2 * tokens * (units + width) + 6 * 4 * units * width,
    )
    return pl.pallas_call(
        adamw_kernel,
        grid=(units // tile,),
        in_specs=[
            pl.BlockSpec((tokens, tile), lambda i: (0, i)),
            pl.BlockSpec((tokens, width), lambda i: (0, 0)),
            state,
            state,
            state,
        ],
        out_specs=[state, state, state],
        out_shape=[shape, shape, shape],
        cost_estimate=cost,
    )(gathered, cotangent_all, master, moment, second)


def psum_steps(value, axes):
    for axis in reversed(axes):
        value = lax.psum(value, axis)
    return value


def per_device(hidden, residual, master, moment, second, gain, head, lengths, labels):
    t_index = lax.axis_index(TP_AXES)
    block_rows = residual.shape[0]
    weights = master.astype(jnp.bfloat16)
    gathered = lax.all_gather(hidden, DP_AXES, axis=0, tiled=True)
    partial_value = jnp.dot(gathered, weights, preferred_element_type=jnp.float32)
    n_tp = partial_value.shape[0] // block_rows
    mine = (jnp.arange(n_tp, dtype=jnp.int32) == t_index)[:, None, None]
    resid_rows = jnp.where(mine, residual.astype(jnp.float32)[None], 0.0)
    term = partial_value + resid_rows.reshape(partial_value.shape)
    w_vec = gain * head
    stream = lax.psum_scatter(
        term.astype(jnp.bfloat16), TP_AXES, scatter_dimension=0, tiled=True
    ).astype(jnp.float32)
    squares = jnp.sum(stream * stream, 1)
    product = jnp.sum(stream * w_vec[None, :], 1)
    squares, product = exchange_sum(jnp.stack([squares, product]), DP_PARTS)

    seqs_here = block_rows // LEN
    pairs_here = seqs_here // 2
    lens_flat = lengths.reshape(-1)
    lens_here = lax.dynamic_slice_in_dim(lens_flat, t_index * seqs_here, seqs_here, 0)
    labels_here = lax.dynamic_slice_in_dim(labels, t_index * pairs_here, pairs_here, 0)
    position = jnp.arange(LEN, dtype=jnp.int32)
    valid = position[None, :] < lens_here[:, None]
    rstd = lax.rsqrt(squares / D + EPS_NORM)
    score = (rstd * product).reshape(seqs_here, LEN)
    seq_total = jnp.sum(jnp.where(valid, score, 0.0), 1)
    reward = (seq_total / lens_here.astype(jnp.float32)).reshape(pairs_here, 2)
    chosen = jnp.where(labels_here == 1, reward[:, 1], reward[:, 0])
    other = jnp.where(labels_here == 1, reward[:, 0], reward[:, 1])
    margin = chosen - other
    loss = psum_steps(jnp.sum(jax.nn.softplus(-margin)), TP_AXES)
    sig = jax.nn.sigmoid(-margin)
    first = jnp.where(labels_here == 0, -sig, sig)
    dreward = jnp.stack([first, -first], 1).reshape(-1)
    coef = jnp.where(valid, (dreward / lens_here.astype(jnp.float32))[:, None], 0.0).reshape(-1)
    cotangent = (
        coef[:, None] * (rstd[:, None] * w_vec[None, :] - (product * rstd**3 / D)[:, None] * stream)
    ).astype(jnp.bfloat16)
    cotangent_all = lax.all_gather(cotangent, TP_AXES, axis=0, tiled=True)
    new_master, new_moment, new_second = grad_step(gathered, cotangent_all, master, moment, second)
    return (new_master, new_moment, new_second, loss)


def solution(mesh):
    sizes = tuple(size for _, size in DP_PARTS + TP_PARTS)
    fine = Mesh(np.asarray(mesh.devices).reshape(sizes), DP_AXES + TP_AXES)
    two = P(DP_AXES, TP_AXES)
    swapped = P(TP_AXES, DP_AXES)
    return jax.shard_map(
        per_device,
        mesh=fine,
        in_specs=(
            two,
            swapped,
            swapped,
            swapped,
            swapped,
            P(DP_AXES),
            P(DP_AXES),
            P(),
            P(),
        ),
        out_specs=(swapped, swapped, swapped, P()),
        check_vma=False,
    )
```

```python
import jax
import jax.numpy as jnp
import numpy as np
from jax import lax
from jax.experimental import pallas as pl
from jax.experimental.layout import Layout, with_layout_constraint
from jax.sharding import Mesh
from jax.sharding import PartitionSpec as P

D = 8192
LEN = 128
STEP = 100


EPS_NORM = 1e-05

DP_PARTS = (("z_hi", 2), ("y", 4), ("core", 2))
TP_PARTS = (("z_lo", 4), ("x", 4))
DP_AXES = tuple(name for name, _ in DP_PARTS)
TP_AXES = tuple(name for name, _ in TP_PARTS)


def exchange_sum(value, parts):
    for name, size in reversed(parts):
        bit = 1
        while bit < size:
            pairs = [(i, i ^ bit) for i in range(size)]
            value = value + lax.ppermute(value, name, pairs)
            bit *= 2
    return value


def adamw_kernel(hid_ref, cot_ref, master_ref, moment_ref, second_ref, out_master, out_moment, out_second):
    n_blocks, width, rows = cot_ref.shape
    acc = jnp.zeros((width, hid_ref.shape[1]), jnp.float32)
    for r in range(n_blocks):
        acc = acc + jnp.dot(
            cot_ref[r], hid_ref[pl.ds(r * rows, rows), :], preferred_element_type=jnp.float32
        )
    grad = acc.T
    master = master_ref[...]
    new_moment = 0.9 * moment_ref[...] + 0.1 * grad
    new_second = 0.95 * second_ref[...] + 0.05 * grad * grad
    m_hat = new_moment / (1.0 - 0.9**STEP)
    v_hat = new_second / (1.0 - 0.95**STEP)
    out_master[...] = master - 0.001 * (m_hat / (jnp.sqrt(v_hat) + 1e-08) + 0.1 * master)
    out_moment[...] = new_moment
    out_second[...] = new_second


def grad_step(gathered, cotangent_t, master, moment, second, tile=128):
    tokens, units = gathered.shape
    n_blocks, width, rows = cotangent_t.shape
    state = pl.BlockSpec((tile, width), lambda i: (i, 0))
    shape = jax.ShapeDtypeStruct((units, width), jnp.float32)
    cost = pl.CostEstimate(
        flops=2 * tokens * units * width,
        transcendentals=units * width,
        bytes_accessed=2 * tokens * (units + width) + 6 * 4 * units * width,
    )
    return pl.pallas_call(
        adamw_kernel,
        grid=(units // tile,),
        in_specs=[
            pl.BlockSpec((tokens, tile), lambda i: (0, i)),
            pl.BlockSpec((n_blocks, width, rows), lambda i: (0, 0, 0)),
            state,
            state,
            state,
        ],
        out_specs=[state, state, state],
        out_shape=[shape, shape, shape],
        cost_estimate=cost,
    )(gathered, cotangent_t, master, moment, second)


def psum_steps(value, axes):
    for axis in reversed(axes):
        value = lax.psum(value, axis)
    return value


def per_device(hidden, residual, master, moment, second, gain, head, lengths, labels):
    t_index = lax.axis_index(TP_AXES)
    block_rows = residual.shape[0]
    weights = master.astype(jnp.bfloat16)
    gathered = lax.all_gather(hidden, DP_AXES, axis=0, tiled=True)
    partial_value = jnp.dot(gathered, weights, preferred_element_type=jnp.float32)
    n_tp = partial_value.shape[0] // block_rows
    mine = (jnp.arange(n_tp, dtype=jnp.int32) == t_index)[:, None, None]
    resid_rows = jnp.where(mine, residual.astype(jnp.float32)[None], 0.0)
    term = partial_value + resid_rows.reshape(partial_value.shape)
    w_vec = gain * head
    stream = lax.psum_scatter(
        term.astype(jnp.bfloat16), TP_AXES, scatter_dimension=0, tiled=True
    ).astype(jnp.float32)
    squares = jnp.sum(stream * stream, 1)
    product = jnp.sum(stream * w_vec[None, :], 1)
    squares, product = exchange_sum(jnp.stack([squares, product]), DP_PARTS)

    seqs_here = block_rows // LEN
    pairs_here = seqs_here // 2
    lens_flat = lengths.reshape(-1)
    lens_here = lax.dynamic_slice_in_dim(lens_flat, t_index * seqs_here, seqs_here, 0)
    labels_here = lax.dynamic_slice_in_dim(labels, t_index * pairs_here, pairs_here, 0)
    position = jnp.arange(LEN, dtype=jnp.int32)
    valid = position[None, :] < lens_here[:, None]
    rstd = lax.rsqrt(squares / D + EPS_NORM)
    score = (rstd * product).reshape(seqs_here, LEN)
    seq_total = jnp.sum(jnp.where(valid, score, 0.0), 1)
    reward = (seq_total / lens_here.astype(jnp.float32)).reshape(pairs_here, 2)
    chosen = jnp.where(labels_here == 1, reward[:, 1], reward[:, 0])
    other = jnp.where(labels_here == 1, reward[:, 0], reward[:, 1])
    margin = chosen - other
    loss = psum_steps(jnp.sum(jax.nn.softplus(-margin)), TP_AXES)
    sig = jax.nn.sigmoid(-margin)
    first = jnp.where(labels_here == 0, -sig, sig)
    dreward = jnp.stack([first, -first], 1).reshape(-1)
    coef = jnp.where(valid, (dreward / lens_here.astype(jnp.float32))[:, None], 0.0).reshape(-1)
    cotangent = (
        coef[:, None] * (rstd[:, None] * w_vec[None, :] - (product * rstd**3 / D)[:, None] * stream)
    ).astype(jnp.bfloat16)
    block_t = with_layout_constraint(cotangent.T, Layout(major_to_minor=(0, 1)))
    cotangent_t = lax.all_gather(block_t, TP_AXES, axis=0, tiled=False)
    new_master, new_moment, new_second = grad_step(gathered, cotangent_t, master, moment, second)
    return (new_master, new_moment, new_second, loss)


def solution(mesh):
    sizes = tuple(size for _, size in DP_PARTS + TP_PARTS)
    fine = Mesh(np.asarray(mesh.devices).reshape(sizes), DP_AXES + TP_AXES)
    two = P(DP_AXES, TP_AXES)
    swapped = P(TP_AXES, DP_AXES)
    return jax.shard_map(
        per_device,
        mesh=fine,
        in_specs=(
            two,
            swapped,
            swapped,
            swapped,
            swapped,
            P(DP_AXES),
            P(DP_AXES),
            P(),
            P(),
        ),
        out_specs=(swapped, swapped, swapped, P()),
        check_vma=False,
    )
```

```python
import jax
import jax.numpy as jnp
import numpy as np
from jax import lax
from jax.experimental.layout import Layout, with_layout_constraint
from jax.sharding import Mesh
from jax.sharding import PartitionSpec as P

D = 8192
LEN = 128
STEP = 100


EPS_NORM = 1e-05

DP_PARTS = (("z_hi", 2), ("y", 4), ("core", 2))
TP_PARTS = (("z_lo", 4), ("x", 4))
DP_AXES = tuple(name for name, _ in DP_PARTS)
TP_AXES = tuple(name for name, _ in TP_PARTS)


def exchange_sum(value):
    pairs = [(c * 4 + z, (1 - c) * 4 + (z ^ 2)) for c in range(2) for z in range(4)]
    value = value + lax.ppermute(value, ("core", "z_lo"), pairs)
    for name, size in (("y", 4), ("z_hi", 2)):
        bit = 1
        while bit < size:
            value = value + lax.ppermute(value, name, [(i, i ^ bit) for i in range(size)])
            bit *= 2
    return value


def psum_steps(value, axes):
    for axis in reversed(axes):
        value = lax.psum(value, axis)
    return value


def per_device(hidden, residual, master, moment, second, gain, head, lengths, labels):
    t_index = lax.axis_index(TP_AXES)
    core = lax.axis_index("core")
    block_rows = residual.shape[0]
    weights = master.astype(jnp.bfloat16)
    chip_axes = DP_AXES[:-1]
    mine_first = lax.all_gather(hidden, chip_axes, axis=0, tiled=True)
    other = lax.ppermute(mine_first, "core", [(0, 1), (1, 0)])
    halves = (mine_first, other)
    n_chips = mine_first.shape[0] // block_rows
    chip_ids = jnp.arange(n_chips, dtype=jnp.int32)
    order = jnp.concatenate([chip_ids * 2 + core, chip_ids * 2 + 1 - core])
    terms = []
    for h, rows in enumerate(halves):
        value = jnp.dot(rows, weights, preferred_element_type=jnp.float32)
        mine = (order[h * n_chips:(h + 1) * n_chips] == t_index)[:, None, None]
        resid_rows = jnp.where(mine, residual.astype(jnp.float32)[None], 0.0)
        terms.append((value + resid_rows.reshape(value.shape)).astype(jnp.bfloat16))
    term = jnp.concatenate(terms, 0)
    own_block = order[t_index]
    w_vec = gain * head
    stream = lax.psum_scatter(term, TP_AXES, scatter_dimension=0, tiled=True).astype(jnp.float32)
    squares = jnp.sum(stream * stream, 1)
    product = jnp.sum(stream * w_vec[None, :], 1)
    squares, product = exchange_sum(jnp.stack([squares, product]))

    seqs_here = block_rows // LEN
    pairs_here = seqs_here // 2
    lens_flat = lengths.reshape(-1)
    lens_here = lax.dynamic_slice_in_dim(lens_flat, own_block * seqs_here, seqs_here, 0)
    labels_here = lax.dynamic_slice_in_dim(labels, own_block * pairs_here, pairs_here, 0)
    position = jnp.arange(LEN, dtype=jnp.int32)
    valid = position[None, :] < lens_here[:, None]
    rstd = lax.rsqrt(squares / D + EPS_NORM)
    score = (rstd * product).reshape(seqs_here, LEN)
    seq_total = jnp.sum(jnp.where(valid, score, 0.0), 1)
    reward = (seq_total / lens_here.astype(jnp.float32)).reshape(pairs_here, 2)
    chosen = jnp.where(labels_here == 1, reward[:, 1], reward[:, 0])
    other = jnp.where(labels_here == 1, reward[:, 0], reward[:, 1])
    margin = chosen - other
    n_pairs = labels.shape[0]
    slots = jnp.zeros((n_pairs,), jnp.float32)
    slots = lax.dynamic_update_slice_in_dim(slots, jax.nn.softplus(-margin), own_block * pairs_here, 0)
    slots = psum_steps(slots, TP_AXES)
    loss = slots[0]
    for p in range(1, n_pairs):
        loss = loss + slots[p]
    sig = jax.nn.sigmoid(-margin)
    first = jnp.where(labels_here == 0, -sig, sig)
    dreward = jnp.stack([first, -first], 1).reshape(-1)
    coef = jnp.where(valid, (dreward / lens_here.astype(jnp.float32))[:, None], 0.0).reshape(-1)
    cotangent = (
        coef[:, None] * (rstd[:, None] * w_vec[None, :] - (product * rstd**3 / D)[:, None] * stream)
    ).astype(jnp.bfloat16)
    cotangent_all = lax.all_gather(cotangent, TP_AXES, axis=0, tiled=True)
    contract = (((0,), (0,)), ((), ()))
    half_rows = mine_first.shape[0]
    grad = sum(
        lax.dot_general(
            rows,
            cotangent_all[h * half_rows:(h + 1) * half_rows],
            contract,
            preferred_element_type=jnp.float32,
        )
        for h, rows in enumerate(halves)
    )
    grad = with_layout_constraint(grad, Layout(major_to_minor=(0, 1)))
    new_moment = 0.9 * moment + 0.1 * grad
    new_second = 0.95 * second + 0.05 * grad * grad
    m_hat = new_moment / (1.0 - 0.9**STEP)
    v_hat = new_second / (1.0 - 0.95**STEP)
    new_master = master - 0.001 * (m_hat / (jnp.sqrt(v_hat) + 1e-08) + 0.1 * master)
    return (new_master, new_moment, new_second, loss)


def solution(mesh):
    sizes = tuple(size for _, size in DP_PARTS + TP_PARTS)
    fine = Mesh(np.asarray(mesh.devices).reshape(sizes), DP_AXES + TP_AXES)
    two = P(DP_AXES, TP_AXES)
    swapped = P(TP_AXES, DP_AXES)
    return jax.shard_map(
        per_device,
        mesh=fine,
        in_specs=(
            two,
            swapped,
            swapped,
            swapped,
            swapped,
            P(DP_AXES),
            P(DP_AXES),
            P(),
            P(),
        ),
        out_specs=(swapped, swapped, swapped, P()),
        check_vma=False,
    )
```

```python
import jax
import jax.numpy as jnp
import numpy as np
from jax import lax
from jax.experimental import pallas as pl
from jax.experimental.layout import Layout, with_layout_constraint
from jax.sharding import Mesh
from jax.sharding import PartitionSpec as P

D = 8192
LEN = 128
STEP = 100


EPS_NORM = 1e-05

DP_PARTS = (("z_hi", 2), ("y", 4), ("core", 2))
TP_PARTS = (("z_lo", 4), ("x", 4))
DP_AXES = tuple(name for name, _ in DP_PARTS)
TP_AXES = tuple(name for name, _ in TP_PARTS)


def exchange_sum(value, parts):
    for name, size in reversed(parts):
        bit = 1
        while bit < size:
            pairs = [(i, i ^ bit) for i in range(size)]
            value = value + lax.ppermute(value, name, pairs)
            bit *= 2
    return value


def adamw_kernel(hid_ref, cot_ref, master_ref, moment_ref, second_ref, out_master, out_moment, out_second):
    grad = jnp.dot(hid_ref[...], cot_ref[...], preferred_element_type=jnp.float32)
    master = master_ref[...]
    new_moment = 0.9 * moment_ref[...] + 0.1 * grad
    new_second = 0.95 * second_ref[...] + 0.05 * grad * grad
    m_hat = new_moment / (1.0 - 0.9**STEP)
    v_hat = new_second / (1.0 - 0.95**STEP)
    out_master[...] = master - 0.001 * (m_hat / (jnp.sqrt(v_hat) + 1e-08) + 0.1 * master)
    out_moment[...] = new_moment
    out_second[...] = new_second


def grad_step(gathered_t, cotangent_all, master, moment, second, tile=128):
    units, tokens = gathered_t.shape
    width = cotangent_all.shape[1]
    state = pl.BlockSpec((tile, width), lambda i: (i, 0))
    shape = jax.ShapeDtypeStruct((units, width), jnp.float32)
    cost = pl.CostEstimate(
        flops=2 * tokens * units * width,
        transcendentals=units * width,
        bytes_accessed=2 * tokens * (units + width) + 6 * 4 * units * width,
    )
    return pl.pallas_call(
        adamw_kernel,
        grid=(units // tile,),
        in_specs=[
            pl.BlockSpec((tile, tokens), lambda i: (i, 0)),
            pl.BlockSpec((tokens, width), lambda i: (0, 0)),
            state,
            state,
            state,
        ],
        out_specs=[state, state, state],
        out_shape=[shape, shape, shape],
        cost_estimate=cost,
    )(gathered_t, cotangent_all, master, moment, second)


def psum_steps(value, axes):
    for axis in reversed(axes):
        value = lax.psum(value, axis)
    return value


def per_device(hidden, residual, master, moment, second, gain, head, lengths, labels):
    t_index = lax.axis_index(TP_AXES)
    block_rows = residual.shape[0]
    weights = master.astype(jnp.bfloat16)
    gathered = lax.all_gather(hidden, DP_AXES, axis=0, tiled=True)
    partial_value = jnp.dot(gathered, weights, preferred_element_type=jnp.float32)
    n_tp = partial_value.shape[0] // block_rows
    mine = (jnp.arange(n_tp, dtype=jnp.int32) == t_index)[:, None, None]
    resid_rows = jnp.where(mine, residual.astype(jnp.float32)[None], 0.0)
    term = partial_value + resid_rows.reshape(partial_value.shape)
    w_vec = gain * head
    stream = lax.psum_scatter(
        term.astype(jnp.bfloat16), TP_AXES, scatter_dimension=0, tiled=True
    ).astype(jnp.float32)
    squares = jnp.sum(stream * stream, 1)
    product = jnp.sum(stream * w_vec[None, :], 1)
    squares, product = exchange_sum(jnp.stack([squares, product]), DP_PARTS)

    seqs_here = block_rows // LEN
    pairs_here = seqs_here // 2
    lens_flat = lengths.reshape(-1)
    lens_here = lax.dynamic_slice_in_dim(lens_flat, t_index * seqs_here, seqs_here, 0)
    labels_here = lax.dynamic_slice_in_dim(labels, t_index * pairs_here, pairs_here, 0)
    position = jnp.arange(LEN, dtype=jnp.int32)
    valid = position[None, :] < lens_here[:, None]
    rstd = lax.rsqrt(squares / D + EPS_NORM)
    score = (rstd * product).reshape(seqs_here, LEN)
    seq_total = jnp.sum(jnp.where(valid, score, 0.0), 1)
    reward = (seq_total / lens_here.astype(jnp.float32)).reshape(pairs_here, 2)
    chosen = jnp.where(labels_here == 1, reward[:, 1], reward[:, 0])
    other = jnp.where(labels_here == 1, reward[:, 0], reward[:, 1])
    margin = chosen - other
    loss = psum_steps(jnp.sum(jax.nn.softplus(-margin)), TP_AXES)
    sig = jax.nn.sigmoid(-margin)
    first = jnp.where(labels_here == 0, -sig, sig)
    dreward = jnp.stack([first, -first], 1).reshape(-1)
    coef = jnp.where(valid, (dreward / lens_here.astype(jnp.float32))[:, None], 0.0).reshape(-1)
    cotangent = (
        coef[:, None] * (rstd[:, None] * w_vec[None, :] - (product * rstd**3 / D)[:, None] * stream)
    ).astype(jnp.bfloat16)
    cotangent_all = lax.all_gather(cotangent, TP_AXES, axis=0, tiled=True)
    gathered_t = with_layout_constraint(gathered.T, Layout(major_to_minor=(0, 1)))
    new_master, new_moment, new_second = grad_step(gathered_t, cotangent_all, master, moment, second)
    return (new_master, new_moment, new_second, loss)


def solution(mesh):
    sizes = tuple(size for _, size in DP_PARTS + TP_PARTS)
    fine = Mesh(np.asarray(mesh.devices).reshape(sizes), DP_AXES + TP_AXES)
    two = P(DP_AXES, TP_AXES)
    swapped = P(TP_AXES, DP_AXES)
    return jax.shard_map(
        per_device,
        mesh=fine,
        in_specs=(
            two,
            swapped,
            swapped,
            swapped,
            swapped,
            P(DP_AXES),
            P(DP_AXES),
            P(),
            P(),
        ),
        out_specs=(swapped, swapped, swapped, P()),
        check_vma=False,
    )
```
